512 devices in a mesh: wide: 32 (over y, z_hi, core), loop: 16 (over z_lo, x).
Axes of the slice: x: 4, y: 8, z: 8 (z_hi: 2, z_lo: 4; z = z_hi * 4 + z_lo), core: 2. Of those that a mesh axis runs over, the one named last changes fastest.
Arguments:
- feats: bfloat16 [16384, 512], P('loop'), may hold values from -6 to 6
- tiles: bfloat16 [16, 32, 4, 128, 128], P('loop', 'wide'), may hold values from -0.1875 to 0.1875
- tile_rows: int32 [16, 32, 4], P('loop', 'wide'), may hold values from 0 to 7
- tile_cols: int32 [16, 32, 4], P('loop', 'wide'), may hold values from 0 to 15
- tile_count: int32 [16, 32], P('loop', 'wide'), may hold values from 1 to 4, as said below
- w_msg: bfloat16 [512, 512], replicated, may hold values from -0.25 to 0.25
- w_self: bfloat16 [512, 512], replicated, may hold values from -0.25 to 0.25
- readout: float32 [512], replicated, may hold values from -0.6 to 0.6
- labels: int32 [16384], P('loop'), may hold values from 0 to 1
Outputs:
- logits: float32 [16384], P('loop')
- grad_msg: bfloat16 [512, 512], replicated
- grad_self: bfloat16 [512, 512], replicated
The draws below stay inside these ranges and needn't reach their ends.
Inputs may be any that keep to these rules, and one draw needn't show every extreme that they name: `tile_count`: some loop and wide index uses all 4 slots in every draw.
All inputs are finite; a program needn't handle non-finite values.
Results may differ from the reference program's by a relative error of at most 0.02.
Values may be sent and summed in bfloat16 or wider, within the bound.
No kernel may reach another device: no remote copies, remote signals or barrier semaphores. Data moves between devices by JAX's collectives and lax.ppermute only.
A program may use at most 64 MiB of HBM per device.

```python
import jax
import jax.numpy as jnp
from jax import lax

D = 512
TB = 128
NODES = 16384
BLOCKS_DEV = 8
COLS_OWN = 1
TILE_DEV = 4
N_WIDE = 32
N_LOOP = 16


def draw_tile_count(key, part):
    low_key, pick_key = jax.random.split(jax.random.fold_in(key, 7))
    counts = jax.random.randint(low_key, (N_LOOP * N_WIDE,), max(1, TILE_DEV // 4), TILE_DEV * 3 // 4 + 1, dtype=jnp.int32)
    busiest = jax.random.randint(pick_key, (), 0, N_LOOP * N_WIDE, dtype=jnp.int32)
    counts = jnp.where(jnp.arange(N_LOOP * N_WIDE, dtype=jnp.int32) == busiest, TILE_DEV, counts)
    return counts.reshape(N_LOOP, N_WIDE).astype(jnp.int32)


def with_ends(result, rng, smallest, top_value):
    longest = result.shape.index(max(result.shape))
    spots = []
    for shift in (0, 1):
        where = [jax.random.randint(jax.random.fold_in(rng, axis), (), 0, length) for axis, length in enumerate(result.shape)]
        where[longest] = (where[longest] + shift) % result.shape[longest]
        spots.append(tuple(where))
    return result.at[spots[0]].set(smallest).at[spots[1]].set(top_value)


def steps_of(key, dims, pieces, low, high):
    loudness = 1.0
    for axis_at, parts in pieces:
        draws = jax.random.uniform(jax.random.fold_in(jax.random.fold_in(key, 6), axis_at), (parts,), jnp.float32, low / len(pieces), high / len(pieces))
        loudness = loudness * jnp.repeat(jnp.exp(draws), dims[axis_at] // parts).reshape((-1,) + (1,) * (len(dims) - 1 - axis_at))
    return loudness


def scatter_about(own_key, shape, width, most, shards=(), held_as=jnp.bfloat16):
    factor_of = steps_of(own_key, shape, shards, -0.22, 0.18) if shards else 1.0
    result = jax.random.normal(own_key, shape, jnp.float32) * width * factor_of
    return jnp.minimum(jnp.maximum(result, -most), most).astype(held_as)


def setup_inputs(seed: int = 0) -> dict:
    streams_of = jax.random.split(jax.random.key(seed), 10)
    feats = scatter_about(streams_of[0], (NODES, D), 1.0, 6.0, ((0, 16),))
    tiles = scatter_about(streams_of[1], (N_LOOP, N_WIDE, TILE_DEV, TB, TB), (8 * TB) ** -0.5, 0.1875, ((0, 16), (1, 32)))
    tile_rows = with_ends(jax.random.randint(streams_of[2], (N_LOOP, N_WIDE, TILE_DEV), 0, BLOCKS_DEV), jax.random.fold_in(streams_of[2], 1), 0, BLOCKS_DEV - 1).astype(jnp.int32)
    tile_cols = with_ends(jax.random.randint(streams_of[3], (N_LOOP, N_WIDE, TILE_DEV), 0, N_LOOP * COLS_OWN), jax.random.fold_in(streams_of[3], 1), 0, (N_LOOP * COLS_OWN) - 1).astype(jnp.int32)
    tile_count = draw_tile_count(jax.random.fold_in(streams_of[9], 71), 0)
    w_msg = scatter_about(streams_of[5], (D, D), D ** -0.5, 0.25)
    w_self = scatter_about(streams_of[6], (D, D), D ** -0.5, 0.25)
    readout = scatter_about(streams_of[7], (D,), 0.1, 0.6, (), jnp.float32)
    labels = with_ends(jax.random.randint(streams_of[8], (NODES,), 0, 2), jax.random.fold_in(streams_of[8], 1), 0, 1).astype(jnp.int32)
    return {"feats": feats, "tiles": tiles, "tile_rows": tile_rows, "tile_cols": tile_cols, "tile_count": tile_count, "w_msg": w_msg, "w_self": w_self, "readout": readout, "labels": labels}


def reference(feats, tiles, tile_rows, tile_cols, tile_count, w_msg, w_self, readout, labels):
    blocks = feats.reshape(N_LOOP, BLOCKS_DEV, TB, D)
    wide_ids = jnp.arange(N_WIDE, dtype=jnp.int32)
    slot_ids = jnp.arange(TILE_DEV, dtype=jnp.int32)
    row_ids = jnp.arange(BLOCKS_DEV, dtype=jnp.int32)

    def one_loop(loop_pos):
        cols_here = tile_cols[loop_pos]
        source = (cols_here // COLS_OWN).astype(jnp.int32)
        sub_block = (cols_here % COLS_OWN).astype(jnp.int32)
        local_block = (wide_ids[:, None] % BLOCKS_DEV + N_WIDE * sub_block).astype(jnp.int32)
        fetched = blocks[source, local_block]
        product = jnp.einsum("wsij,wsjd->wsid", tiles[loop_pos].astype(jnp.float32),
                             fetched.astype(jnp.float32), precision=lax.Precision.HIGHEST)
        valid_slot = slot_ids[None, :] < tile_count[loop_pos][:, None]
        placing = ((tile_rows[loop_pos][:, :, None] == row_ids[None, None, :])
                   & valid_slot[:, :, None]).astype(jnp.float32)
        partial_value = jnp.einsum("wsr,wsid->wrid", placing, product, precision=lax.Precision.HIGHEST)
        partial_value = lax.optimization_barrier(partial_value.astype(jnp.bfloat16))
        return jnp.sum(partial_value.astype(jnp.float32), axis=0).astype(jnp.bfloat16)

    message = lax.map(one_loop, jnp.arange(N_LOOP, dtype=jnp.int32)).reshape(NODES, D)
    pre_act = (jnp.dot(message, w_msg, preferred_element_type=jnp.float32)
               + jnp.dot(feats, w_self, preferred_element_type=jnp.float32))
    hidden = feats.astype(jnp.float32) + jax.nn.silu(pre_act)
    logits = jnp.dot(hidden, readout, precision=lax.Precision.HIGHEST)
    residual_grad = jax.nn.sigmoid(logits) - labels.astype(jnp.float32)
    gate_sig = jax.nn.sigmoid(pre_act)
    pre_grad = (residual_grad[:, None] * readout[None, :] * gate_sig
                * (1.0 + pre_act * (1.0 - gate_sig))).astype(jnp.bfloat16)
    grad_msg = jnp.dot(message.T, pre_grad, preferred_element_type=jnp.float32).astype(jnp.bfloat16)
    grad_self = jnp.dot(feats.T, pre_grad, preferred_element_type=jnp.float32).astype(jnp.bfloat16)
    return (logits, grad_msg, grad_self)
```

```python
import jax
import jax.numpy as jnp
from jax import lax
from jax.sharding import Mesh, PartitionSpec as P


def copy_for_each(value, axis):
    copies = jnp.broadcast_to(value, (lax.axis_size(axis), *value.shape))
    return lax.all_to_all(copies, axis, split_axis=0, concat_axis=0, tiled=True)


def laid_out(blocks, dim):
    shape = list(blocks.shape[1:])
    shape[dim] *= blocks.shape[0]
    return jnp.moveaxis(blocks, 0, dim).reshape(shape)


def gather_directly(value, axis, dim):
    blocks = copy_for_each(value, axis)
    return laid_out(blocks, dim)


def in_blocks(value, dim, devices):
    before, after = (value.shape[:dim], value.shape[dim + 1 :])
    return jnp.moveaxis(value.reshape(*before, devices, -1, *after), dim, 0)


def sum_at_owner(value, axis, dim):
    devices = lax.axis_size(axis)
    blocks = lax.all_to_all(in_blocks(value, dim, devices), axis, 0, 0, tiled=True)
    return jnp.sum(blocks.astype(jnp.float32), axis=0)


WIDE = ("wy", "wz", "wc")


def body(feats, tiles, tile_rows, tile_cols, tile_count, w_msg, w_self, readout, labels):
    rows_dev, feat_width = feats.shape
    size_tb = tiles.shape[-1]
    slot_count = tiles.shape[2]
    blocks_dev = rows_dev // size_tb
    wide_size = lax.axis_size(WIDE)
    cols_own = max(1, blocks_dev // wide_size)
    wide_pos = (lax.axis_index("wy") * lax.axis_size("wz") + lax.axis_index("wz")) * lax.axis_size(
        "wc"
    ) + lax.axis_index("wc")
    picked_blocks = wide_pos % blocks_dev + wide_size * jnp.arange(cols_own, dtype=jnp.int32)
    own_blocks = jnp.take(feats.reshape(blocks_dev, size_tb, feat_width), picked_blocks, axis=0)
    gathered = gather_directly(own_blocks, "loop", 0)
    tile_vals = tiles.reshape(slot_count, size_tb, size_tb)
    chosen = jnp.take(gathered, tile_cols.reshape(slot_count), axis=0)
    product = jnp.einsum("sij,sjd->sid", tile_vals, chosen, preferred_element_type=jnp.float32)
    valid_slot = jnp.arange(slot_count, dtype=jnp.int32) < tile_count.reshape(())
    placing = (
        (tile_rows.reshape(slot_count)[:, None] == jnp.arange(blocks_dev, dtype=jnp.int32)[None, :])
        & valid_slot[:, None]
    ).astype(jnp.float32)
    partial_value = jnp.einsum(
        "sr,sid->rid", placing, product, precision=lax.Precision.HIGHEST
    ).reshape(rows_dev, feat_width)
    core = lax.axis_index("wc")
    by_owner = partial_value.astype(jnp.bfloat16).reshape(
        lax.axis_size("wy"), lax.axis_size("wz"), lax.axis_size("wc"), -1, feat_width
    )
    keep = lax.dynamic_index_in_dim(by_owner, core, 2, keepdims=False)
    give = lax.dynamic_index_in_dim(by_owner, 1 - core, 2, keepdims=False)
    got = lax.ppermute(give, "wc", [(0, 1), (1, 0)])
    pair_sum = (keep.astype(jnp.float32) + got.astype(jnp.float32)).astype(jnp.bfloat16)
    pair_sum = pair_sum.reshape(-1, pair_sum.shape[-2], feat_width)
    message = sum_at_owner(pair_sum, ("wy", "wz"), 0).astype(jnp.bfloat16)
    message = message.reshape(-1, feat_width)
    share_rows = rows_dev // wide_size
    node_feats = lax.dynamic_slice_in_dim(feats, wide_pos * share_rows, share_rows, 0)
    node_labels = lax.dynamic_slice_in_dim(labels, wide_pos * share_rows, share_rows, 0)
    pre_act = jnp.dot(message, w_msg, preferred_element_type=jnp.float32) + jnp.dot(
        node_feats, w_self, preferred_element_type=jnp.float32
    )
    hidden = node_feats.astype(jnp.float32) + jax.nn.silu(pre_act)
    logits = jnp.dot(hidden, readout, precision=lax.Precision.HIGHEST)
    residual_grad = jax.nn.sigmoid(logits) - node_labels.astype(jnp.float32)
    gate_sig = jax.nn.sigmoid(pre_act)
    pre_grad = (
        residual_grad[:, None] * readout[None, :] * gate_sig * (1.0 + pre_act * (1.0 - gate_sig))
    ).astype(jnp.bfloat16)
    grad_msg = jnp.einsum("na,nb->ab", message, pre_grad, preferred_element_type=jnp.float32)
    grad_self = jnp.einsum("na,nb->ab", node_feats, pre_grad, preferred_element_type=jnp.float32)
    grad_msg, grad_self = lax.psum((grad_msg, grad_self), (*WIDE, "loop"))
    out_logits = gather_directly(logits, WIDE, 0)
    return (out_logits, grad_msg.astype(jnp.bfloat16), grad_self.astype(jnp.bfloat16))


def solution(mesh):
    wide_devices, loop_devices = mesh.devices.shape
    split = Mesh(mesh.devices.reshape(wide_devices // 4, 2, 2, loop_devices), (*WIDE, "loop"))
    placed = (
        P("loop", None),
        P("loop", WIDE, None, None, None),
        P("loop", WIDE, None),
        P("loop", WIDE, None),
        P("loop", WIDE),
        P(),
        P(),
        P(),
        P("loop"),
    )
    return jax.shard_map(
        body, mesh=split, in_specs=placed, out_specs=(P("loop"), P(), P()), check_vma=False
    )
```

```python
import jax
import jax.numpy as jnp
from jax import lax
from jax.sharding import Mesh, PartitionSpec as P


def copy_for_each(value, axis):
    copies = jnp.broadcast_to(value, (lax.axis_size(axis), *value.shape))
    return lax.all_to_all(copies, axis, split_axis=0, concat_axis=0, tiled=True)


def laid_out(blocks, dim):
    shape = list(blocks.shape[1:])
    shape[dim] *= blocks.shape[0]
    return jnp.moveaxis(blocks, 0, dim).reshape(shape)


def gather_directly(value, axis, dim):
    blocks = copy_for_each(value, axis)
    return laid_out(blocks, dim)


def in_blocks(value, dim, devices):
    before, after = (value.shape[:dim], value.shape[dim + 1 :])
    return jnp.moveaxis(value.reshape(*before, devices, -1, *after), dim, 0)


def sum_at_owner(value, axis, dim):
    devices = lax.axis_size(axis)
    blocks = lax.all_to_all(in_blocks(value, dim, devices), axis, 0, 0, tiled=True)
    return jnp.sum(blocks.astype(jnp.float32), axis=0)


WIDE = ("wy", "wz", "wc")


def body(feats, tiles, tile_rows, tile_cols, tile_count, w_msg, w_self, readout, labels):
    rows_dev, feat_width = feats.shape
    size_tb = tiles.shape[-1]
    slot_count = tiles.shape[2]
    blocks_dev = rows_dev // size_tb
    wide_size = lax.axis_size(WIDE)
    cols_own = max(1, blocks_dev // wide_size)
    wide_pos = (lax.axis_index("wy") * lax.axis_size("wz") + lax.axis_index("wz")) * lax.axis_size(
        "wc"
    ) + lax.axis_index("wc")
    picked_blocks = wide_pos % blocks_dev + wide_size * jnp.arange(cols_own, dtype=jnp.int32)
    own_blocks = jnp.take(feats.reshape(blocks_dev, size_tb, feat_width), picked_blocks, axis=0)
    gathered = gather_directly(own_blocks, "loop", 0)
    tile_vals = tiles.reshape(slot_count, size_tb, size_tb)
    chosen = jnp.take(gathered, tile_cols.reshape(slot_count), axis=0)
    product = jnp.einsum("sij,sjd->sid", tile_vals, chosen, preferred_element_type=jnp.float32)
    valid_slot = jnp.arange(slot_count, dtype=jnp.int32) < tile_count.reshape(())
    placing = (
        (tile_rows.reshape(slot_count)[:, None] == jnp.arange(blocks_dev, dtype=jnp.int32)[None, :])
        & valid_slot[:, None]
    ).astype(jnp.float32)
    partial_value = jnp.einsum(
        "sr,sid->rid", placing, product, precision=lax.Precision.HIGHEST
    ).reshape(rows_dev, feat_width)
    core = lax.axis_index("wc")
    by_owner = partial_value.astype(jnp.bfloat16).reshape(
        lax.axis_size("wy"), lax.axis_size("wz"), lax.axis_size("wc"), -1, feat_width
    )
    keep = lax.dynamic_index_in_dim(by_owner, core, 2, keepdims=False)
    give = lax.dynamic_index_in_dim(by_owner, 1 - core, 2, keepdims=False)
    got = lax.ppermute(give, "wc", [(0, 1), (1, 0)])
    pair_sum = (keep.astype(jnp.float32) + got.astype(jnp.float32)).astype(jnp.bfloat16)
    pair_sum = pair_sum.reshape(-1, pair_sum.shape[-2], feat_width)
    message = sum_at_owner(pair_sum, ("wy", "wz"), 0).astype(jnp.bfloat16)
    message = message.reshape(-1, feat_width)
    share_rows = rows_dev // wide_size
    node_feats = lax.dynamic_slice_in_dim(feats, wide_pos * share_rows, share_rows, 0)
    node_labels = lax.dynamic_slice_in_dim(labels, wide_pos * share_rows, share_rows, 0)
    pre_act = jnp.dot(message, w_msg, preferred_element_type=jnp.float32) + jnp.dot(
        node_feats, w_self, preferred_element_type=jnp.float32
    )
    hidden = node_feats.astype(jnp.float32) + jax.nn.silu(pre_act)
    logits = jnp.dot(hidden, readout, precision=lax.Precision.HIGHEST)
    residual_grad = jax.nn.sigmoid(logits) - node_labels.astype(jnp.float32)
    gate_sig = jax.nn.sigmoid(pre_act)
    pre_grad = (
        residual_grad[:, None] * readout[None, :] * gate_sig * (1.0 + pre_act * (1.0 - gate_sig))
    ).astype(jnp.bfloat16)
    grad_msg = jnp.einsum("na,nb->ab", message, pre_grad, preferred_element_type=jnp.float32)
    grad_self = jnp.einsum("na,nb->ab", node_feats, pre_grad, preferred_element_type=jnp.float32)
    loop_pos = lax.axis_index("loop")
    all_logits = jnp.zeros((lax.axis_size("loop") * rows_dev,), jnp.float32)
    all_logits = lax.dynamic_update_slice_in_dim(
        all_logits, logits, loop_pos * rows_dev + wide_pos * share_rows, 0
    ).reshape(-1, feat_width)
    logit_hi = all_logits.astype(jnp.bfloat16).astype(jnp.float32)
    logit_rest = all_logits - logit_hi
    logit_mid = logit_rest.astype(jnp.bfloat16).astype(jnp.float32)
    logit_lo = (logit_rest - logit_mid).astype(jnp.bfloat16).astype(jnp.float32)
    msg_rows, self_rows = lax.psum(
        (
            jnp.concatenate([grad_msg, logit_hi, logit_mid], axis=0),
            jnp.concatenate([grad_self, logit_lo], axis=0),
        ),
        (*WIDE, "loop"),
    )
    msg_rows = msg_rows.astype(jnp.bfloat16)
    self_rows = self_rows.astype(jnp.bfloat16)
    parts = logit_hi.shape[0]
    all_logits = (
        msg_rows[feat_width : feat_width + parts].astype(jnp.float32)
        + msg_rows[feat_width + parts :].astype(jnp.float32)
        + self_rows[feat_width:].astype(jnp.float32)
    ).reshape(-1)
    out_logits = lax.dynamic_slice_in_dim(all_logits, loop_pos * rows_dev, rows_dev, 0)
    return (out_logits, msg_rows[:feat_width], self_rows[:feat_width])


def solution(mesh):
    wide_devices, loop_devices = mesh.devices.shape
    split = Mesh(mesh.devices.reshape(wide_devices // 4, 2, 2, loop_devices), (*WIDE, "loop"))
    placed = (
        P("loop", None),
        P("loop", WIDE, None, None, None),
        P("loop", WIDE, None),
        P("loop", WIDE, None),
        P("loop", WIDE),
        P(),
        P(),
        P(),
        P("loop"),
    )
    return jax.shard_map(
        body, mesh=split, in_specs=placed, out_specs=(P("loop"), P(), P()), check_vma=False
    )
```

```python
import jax
import jax.numpy as jnp
from jax import lax
from jax.sharding import Mesh, PartitionSpec as P


def copy_for_each(value, axis):
    copies = jnp.broadcast_to(value, (lax.axis_size(axis), *value.shape))
    return lax.all_to_all(copies, axis, split_axis=0, concat_axis=0, tiled=True)


def laid_out(blocks, dim):
    shape = list(blocks.shape[1:])
    shape[dim] *= blocks.shape[0]
    return jnp.moveaxis(blocks, 0, dim).reshape(shape)


def gather_directly(value, axis, dim):
    blocks = copy_for_each(value, axis)
    return laid_out(blocks, dim)


def in_blocks(value, dim, devices):
    before, after = (value.shape[:dim], value.shape[dim + 1 :])
    return jnp.moveaxis(value.reshape(*before, devices, -1, *after), dim, 0)


def sum_at_owner(value, axis, dim):
    devices = lax.axis_size(axis)
    blocks = lax.all_to_all(in_blocks(value, dim, devices), axis, 0, 0, tiled=True)
    return jnp.sum(blocks.astype(jnp.float32), axis=0)


WIDE = ("wy", "wz", "wc")


def body(feats, tiles, tile_rows, tile_cols, tile_count, w_msg, w_self, readout, labels):
    rows_dev, feat_width = feats.shape
    size_tb = tiles.shape[-1]
    slot_count = tiles.shape[2]
    blocks_dev = rows_dev // size_tb
    wide_size = lax.axis_size(WIDE)
    cols_own = max(1, blocks_dev // wide_size)
    wide_pos = (lax.axis_index("wy") * lax.axis_size("wz") + lax.axis_index("wz")) * lax.axis_size(
        "wc"
    ) + lax.axis_index("wc")
    picked_blocks = wide_pos % blocks_dev + wide_size * jnp.arange(cols_own, dtype=jnp.int32)
    own_blocks = jnp.take(feats.reshape(blocks_dev, size_tb, feat_width), picked_blocks, axis=0)
    gathered = gather_directly(own_blocks, "loop", 0)
    tile_vals = tiles.reshape(slot_count, size_tb, size_tb)
    chosen = jnp.take(gathered, tile_cols.reshape(slot_count), axis=0)
    product = jnp.einsum("sij,sjd->sid", tile_vals, chosen, preferred_element_type=jnp.float32)
    valid_slot = jnp.arange(slot_count, dtype=jnp.int32) < tile_count.reshape(())
    placing = (
        (tile_rows.reshape(slot_count)[:, None] == jnp.arange(blocks_dev, dtype=jnp.int32)[None, :])
        & valid_slot[:, None]
    ).astype(jnp.float32)
    partial_value = jnp.einsum(
        "sr,sid->rid", placing, product, precision=lax.Precision.HIGHEST
    ).reshape(rows_dev, feat_width)
    core = lax.axis_index("wc")
    by_owner = partial_value.astype(jnp.bfloat16).reshape(
        lax.axis_size("wy"), lax.axis_size("wz"), lax.axis_size("wc"), -1, feat_width
    )
    keep = lax.dynamic_index_in_dim(by_owner, core, 2, keepdims=False)
    give = lax.dynamic_index_in_dim(by_owner, 1 - core, 2, keepdims=False)
    got = lax.ppermute(give, "wc", [(0, 1), (1, 0)])
    pair_sum = (keep.astype(jnp.float32) + got.astype(jnp.float32)).astype(jnp.bfloat16)
    pair_sum = pair_sum.reshape(-1, pair_sum.shape[-2], feat_width)
    message = sum_at_owner(pair_sum, ("wy", "wz"), 0).astype(jnp.bfloat16)
    message = message.reshape(-1, feat_width)
    share_rows = rows_dev // wide_size
    node_feats = lax.dynamic_slice_in_dim(feats, wide_pos * share_rows, share_rows, 0)
    node_labels = lax.dynamic_slice_in_dim(labels, wide_pos * share_rows, share_rows, 0)
    pre_act = jnp.dot(message, w_msg, preferred_element_type=jnp.float32) + jnp.dot(
        node_feats, w_self, preferred_element_type=jnp.float32
    )
    hidden = node_feats.astype(jnp.float32) + jax.nn.silu(pre_act)
    logits = jnp.dot(hidden, readout, precision=lax.Precision.HIGHEST)
    residual_grad = jax.nn.sigmoid(logits) - node_labels.astype(jnp.float32)
    gate_sig = jax.nn.sigmoid(pre_act)
    pre_grad = (
        residual_grad[:, None] * readout[None, :] * gate_sig * (1.0 + pre_act * (1.0 - gate_sig))
    ).astype(jnp.bfloat16)
    grad_msg = jnp.einsum("na,nb->ab", message, pre_grad, preferred_element_type=jnp.float32)
    grad_self = jnp.einsum("na,nb->ab", node_feats, pre_grad, preferred_element_type=jnp.float32)
    loop_pos = lax.axis_index("loop")
    all_logits = jnp.zeros((lax.axis_size("loop") * rows_dev,), jnp.float32)
    all_logits = lax.dynamic_update_slice_in_dim(
        all_logits, logits, loop_pos * rows_dev + wide_pos * share_rows, 0
    ).reshape(-1, feat_width)
    logit_hi = all_logits.astype(jnp.bfloat16).astype(jnp.float32)
    logit_rest = all_logits - logit_hi
    logit_mid = logit_rest.astype(jnp.bfloat16).astype(jnp.float32)
    logit_lo = (logit_rest - logit_mid).astype(jnp.bfloat16).astype(jnp.float32)
    logit_parts = jnp.concatenate([logit_hi, logit_mid, logit_lo], axis=0)
    grad_msg, grad_self, logit_parts = lax.psum((grad_msg, grad_self, logit_parts), (*WIDE, "loop"))
    grad_msg = grad_msg.astype(jnp.bfloat16)
    grad_self = grad_self.astype(jnp.bfloat16)
    logit_parts = logit_parts.astype(jnp.bfloat16).astype(jnp.float32).reshape(3, -1)
    all_logits = logit_parts[0] + logit_parts[1] + logit_parts[2]
    out_logits = lax.dynamic_slice_in_dim(all_logits, loop_pos * rows_dev, rows_dev, 0)
    return (out_logits, grad_msg, grad_self)


def solution(mesh):
    wide_devices, loop_devices = mesh.devices.shape
    split = Mesh(mesh.devices.reshape(wide_devices // 4, 2, 2, loop_devices), (*WIDE, "loop"))
    placed = (
        P("loop", None),
        P("loop", WIDE, None, None, None),
        P("loop", WIDE, None),
        P("loop", WIDE, None),
        P("loop", WIDE),
        P(),
        P(),
        P(),
        P("loop"),
    )
    return jax.shard_map(
        body, mesh=split, in_specs=placed, out_specs=(P("loop"), P(), P()), check_vma=False
    )
```

```python
import jax
import jax.numpy as jnp
from jax import lax
from jax.sharding import Mesh, PartitionSpec as P


def copy_for_each(value, axis):
    copies = jnp.broadcast_to(value, (lax.axis_size(axis), *value.shape))
    return lax.all_to_all(copies, axis, split_axis=0, concat_axis=0, tiled=True)


def laid_out(blocks, dim):
    shape = list(blocks.shape[1:])
    shape[dim] *= blocks.shape[0]
    return jnp.moveaxis(blocks, 0, dim).reshape(shape)


def gather_directly(value, axis, dim):
    blocks = copy_for_each(value, axis)
    return laid_out(blocks, dim)


def in_blocks(value, dim, devices):
    before, after = (value.shape[:dim], value.shape[dim + 1 :])
    return jnp.moveaxis(value.reshape(*before, devices, -1, *after), dim, 0)


def sum_at_owner(value, axis, dim):
    devices = lax.axis_size(axis)
    blocks = lax.all_to_all(in_blocks(value, dim, devices), axis, 0, 0, tiled=True)
    return jnp.sum(blocks.astype(jnp.float32), axis=0)


WIDE = ("wy", "wz", "wc")


def body(feats, tiles, tile_rows, tile_cols, tile_count, w_msg, w_self, readout, labels):
    rows_dev, feat_width = feats.shape
    size_tb = tiles.shape[-1]
    slot_count = tiles.shape[2]
    blocks_dev = rows_dev // size_tb
    wide_size = lax.axis_size(WIDE)
    cols_own = max(1, blocks_dev // wide_size)
    wide_pos = (lax.axis_index("wy") * lax.axis_size("wz") + lax.axis_index("wz")) * lax.axis_size(
        "wc"
    ) + lax.axis_index("wc")
    picked_blocks = wide_pos % blocks_dev + wide_size * jnp.arange(cols_own, dtype=jnp.int32)
    own_blocks = jnp.take(feats.reshape(blocks_dev, size_tb, feat_width), picked_blocks, axis=0)
    gathered = gather_directly(own_blocks, "loop", 0)
    tile_vals = tiles.reshape(slot_count, size_tb, size_tb)
    chosen = jnp.take(gathered, tile_cols.reshape(slot_count), axis=0)
    product = jnp.einsum("sij,sjd->sid", tile_vals, chosen, preferred_element_type=jnp.float32)
    valid_slot = jnp.arange(slot_count, dtype=jnp.int32) < tile_count.reshape(())
    placing = (
        (tile_rows.reshape(slot_count)[:, None] == jnp.arange(blocks_dev, dtype=jnp.int32)[None, :])
        & valid_slot[:, None]
    ).astype(jnp.float32)
    partial_value = jnp.einsum(
        "sr,sid->rid", placing, product, precision=lax.Precision.HIGHEST
    ).reshape(rows_dev, feat_width)
    core = lax.axis_index("wc")
    by_owner = partial_value.astype(jnp.bfloat16).reshape(
        lax.axis_size("wy"), lax.axis_size("wz"), lax.axis_size("wc"), -1, feat_width
    )
    keep = lax.dynamic_index_in_dim(by_owner, core, 2, keepdims=False)
    give = lax.dynamic_index_in_dim(by_owner, 1 - core, 2, keepdims=False)
    got = lax.ppermute(give, "wc", [(0, 1), (1, 0)])
    pair_sum = (keep.astype(jnp.float32) + got.astype(jnp.float32)).astype(jnp.bfloat16)
    half = lax.axis_index("wz")
    keep = lax.dynamic_index_in_dim(pair_sum, half, 1, keepdims=False)
    give = lax.dynamic_index_in_dim(pair_sum, 1 - half, 1, keepdims=False)
    got = lax.ppermute(give, "wz", [(0, 1), (1, 0)])
    quad_sum = (keep.astype(jnp.float32) + got.astype(jnp.float32)).astype(jnp.bfloat16)
    message = sum_at_owner(quad_sum, "wy", 0).astype(jnp.bfloat16)
    message = message.reshape(-1, feat_width)
    share_rows = rows_dev // wide_size
    node_feats = lax.dynamic_slice_in_dim(feats, wide_pos * share_rows, share_rows, 0)
    node_labels = lax.dynamic_slice_in_dim(labels, wide_pos * share_rows, share_rows, 0)
    pre_act = jnp.dot(message, w_msg, preferred_element_type=jnp.float32) + jnp.dot(
        node_feats, w_self, preferred_element_type=jnp.float32
    )
    hidden = node_feats.astype(jnp.float32) + jax.nn.silu(pre_act)
    logits = jnp.dot(hidden, readout, precision=lax.Precision.HIGHEST)
    residual_grad = jax.nn.sigmoid(logits) - node_labels.astype(jnp.float32)
    gate_sig = jax.nn.sigmoid(pre_act)
    pre_grad = (
        residual_grad[:, None] * readout[None, :] * gate_sig * (1.0 + pre_act * (1.0 - gate_sig))
    ).astype(jnp.bfloat16)
    grad_msg = jnp.einsum("na,nb->ab", message, pre_grad, preferred_element_type=jnp.float32)
    grad_self = jnp.einsum("na,nb->ab", node_feats, pre_grad, preferred_element_type=jnp.float32)
    loop_pos = lax.axis_index("loop")
    all_logits = jnp.zeros((lax.axis_size("loop") * rows_dev,), jnp.float32)
    all_logits = lax.dynamic_update_slice_in_dim(
        all_logits, logits, loop_pos * rows_dev + wide_pos * share_rows, 0
    ).reshape(-1, feat_width)
    logit_hi = all_logits.astype(jnp.bfloat16).astype(jnp.float32)
    logit_rest = all_logits - logit_hi
    logit_mid = logit_rest.astype(jnp.bfloat16).astype(jnp.float32)
    logit_lo = (logit_rest - logit_mid).astype(jnp.bfloat16).astype(jnp.float32)
    logit_parts = jnp.concatenate([logit_hi, logit_mid, logit_lo], axis=0)
    grad_msg, grad_self, logit_parts = lax.psum((grad_msg, grad_self, logit_parts), (*WIDE, "loop"))
    grad_msg = grad_msg.astype(jnp.bfloat16)
    grad_self = grad_self.astype(jnp.bfloat16)
    logit_parts = logit_parts.astype(jnp.bfloat16).astype(jnp.float32).reshape(3, -1)
    all_logits = logit_parts[0] + logit_parts[1] + logit_parts[2]
    out_logits = lax.dynamic_slice_in_dim(all_logits, loop_pos * rows_dev, rows_dev, 0)
    return (out_logits, grad_msg, grad_self)


def solution(mesh):
    wide_devices, loop_devices = mesh.devices.shape
    split = Mesh(mesh.devices.reshape(wide_devices // 4, 2, 2, loop_devices), (*WIDE, "loop"))
    placed = (
        P("loop", None),
        P("loop", WIDE, None, None, None),
        P("loop", WIDE, None),
        P("loop", WIDE, None),
        P("loop", WIDE),
        P(),
        P(),
        P(),
        P("loop"),
    )
    return jax.shard_map(
        body, mesh=split, in_specs=placed, out_specs=(P("loop"), P(), P()), check_vma=False
    )
```

```python
import jax
import jax.numpy as jnp
from jax import lax
from jax.sharding import Mesh, PartitionSpec as P


def copy_for_each(value, axis):
    copies = jnp.broadcast_to(value, (lax.axis_size(axis), *value.shape))
    return lax.all_to_all(copies, axis, split_axis=0, concat_axis=0, tiled=True)


def laid_out(blocks, dim):
    shape = list(blocks.shape[1:])
    shape[dim] *= blocks.shape[0]
    return jnp.moveaxis(blocks, 0, dim).reshape(shape)


def gather_directly(value, axis, dim):
    blocks = copy_for_each(value, axis)
    return laid_out(blocks, dim)


def in_blocks(value, dim, devices):
    before, after = (value.shape[:dim], value.shape[dim + 1 :])
    return jnp.moveaxis(value.reshape(*before, devices, -1, *after), dim, 0)


def sum_at_owner(value, axis, dim):
    devices = lax.axis_size(axis)
    blocks = lax.all_to_all(in_blocks(value, dim, devices), axis, 0, 0, tiled=True)
    return jnp.sum(blocks.astype(jnp.float32), axis=0)


WIDE = ("wy", "wz", "wc")


def body(feats, tiles, tile_rows, tile_cols, tile_count, w_msg, w_self, readout, labels):
    rows_dev, feat_width = feats.shape
    size_tb = tiles.shape[-1]
    slot_count = tiles.shape[2]
    blocks_dev = rows_dev // size_tb
    wide_size = lax.axis_size(WIDE)
    cols_own = max(1, blocks_dev // wide_size)
    wide_pos = (lax.axis_index("wy") * lax.axis_size("wz") + lax.axis_index("wz")) * lax.axis_size(
        "wc"
    ) + lax.axis_index("wc")
    picked_blocks = wide_pos % blocks_dev + wide_size * jnp.arange(cols_own, dtype=jnp.int32)
    own_blocks = jnp.take(feats.reshape(blocks_dev, size_tb, feat_width), picked_blocks, axis=0)
    gathered = gather_directly(own_blocks, "loop", 0)
    tile_vals = tiles.reshape(slot_count, size_tb, size_tb)
    chosen = jnp.take(gathered, tile_cols.reshape(slot_count), axis=0)
    product = jnp.einsum("sij,sjd->sid", tile_vals, chosen, preferred_element_type=jnp.float32)
    valid_slot = jnp.arange(slot_count, dtype=jnp.int32) < tile_count.reshape(())
    placing = (
        (tile_rows.reshape(slot_count)[:, None] == jnp.arange(blocks_dev, dtype=jnp.int32)[None, :])
        & valid_slot[:, None]
    ).astype(jnp.float32)
    partial_value = jnp.einsum(
        "sr,sid->rid", placing, product, precision=lax.Precision.HIGHEST
    ).reshape(rows_dev, feat_width)
    core = lax.axis_index("wc")
    by_owner = partial_value.astype(jnp.bfloat16).reshape(
        lax.axis_size("wy"), lax.axis_size("wz"), lax.axis_size("wc"), -1, feat_width
    )
    keep = lax.dynamic_index_in_dim(by_owner, core, 2, keepdims=False)
    give = lax.dynamic_index_in_dim(by_owner, 1 - core, 2, keepdims=False)
    got = lax.ppermute(give, "wc", [(0, 1), (1, 0)])
    pair_sum = (keep.astype(jnp.float32) + got.astype(jnp.float32)).astype(jnp.bfloat16)
    pair_sum = pair_sum.reshape(-1, pair_sum.shape[-2], feat_width)
    message = sum_at_owner(pair_sum, ("wy", "wz"), 0).astype(jnp.bfloat16)
    message = message.reshape(-1, feat_width)
    share_rows = rows_dev // wide_size
    node_feats = lax.dynamic_slice_in_dim(feats, wide_pos * share_rows, share_rows, 0)
    node_labels = lax.dynamic_slice_in_dim(labels, wide_pos * share_rows, share_rows, 0)
    pre_act = jnp.dot(message, w_msg, preferred_element_type=jnp.float32) + jnp.dot(
        node_feats, w_self, preferred_element_type=jnp.float32
    )
    hidden = node_feats.astype(jnp.float32) + jax.nn.silu(pre_act)
    logits = jnp.dot(hidden, readout, precision=lax.Precision.HIGHEST)
    residual_grad = jax.nn.sigmoid(logits) - node_labels.astype(jnp.float32)
    gate_sig = jax.nn.sigmoid(pre_act)
    pre_grad = (
        residual_grad[:, None] * readout[None, :] * gate_sig * (1.0 + pre_act * (1.0 - gate_sig))
    ).astype(jnp.bfloat16)
    grad_msg = jnp.einsum("na,nb->ab", message, pre_grad, preferred_element_type=jnp.float32)
    grad_self = jnp.einsum("na,nb->ab", node_feats, pre_grad, preferred_element_type=jnp.float32)
    swap = [(0, 1), (1, 0)]
    others = ("wy", "wz", "loop")
    peers = lax.axis_size(others)
    both_grads = jnp.stack([grad_msg, grad_self]).reshape(2, -1)
    mine = lax.dynamic_index_in_dim(both_grads, core, 0, keepdims=False)
    theirs = lax.dynamic_index_in_dim(both_grads, 1 - core, 0, keepdims=False)
    half_sum = mine + lax.ppermute(theirs, "wc", swap)
    pieces = lax.all_to_all(half_sum.astype(jnp.bfloat16).reshape(peers, -1), others, 0, 0, tiled=True)
    reduced = jnp.sum(pieces.astype(jnp.float32), axis=0).astype(jnp.bfloat16)
    logit_hi = logits.astype(jnp.bfloat16)
    logit_rest = logits - logit_hi.astype(jnp.float32)
    logit_mid = logit_rest.astype(jnp.bfloat16)
    logit_lo = (logit_rest - logit_mid.astype(jnp.float32)).astype(jnp.bfloat16)
    payload = jnp.concatenate([reduced, logit_hi, logit_mid, logit_lo])
    gathered = lax.all_to_all(jnp.broadcast_to(payload, (peers, payload.size)), others, 0, 0, tiled=True)
    from_sibling = lax.ppermute(gathered, "wc", swap)
    by_core = jnp.where(core == 0, jnp.stack([gathered, from_sibling]), jnp.stack([from_sibling, gathered]))
    chunk = reduced.size
    grads = by_core[:, :, :chunk].reshape(2, feat_width, feat_width)
    parts = by_core[:, :, chunk:].reshape(
        2, lax.axis_size("wy"), lax.axis_size("wz"), lax.axis_size("loop"), 3, share_rows
    )
    parts = lax.dynamic_index_in_dim(parts, lax.axis_index("loop"), 3, keepdims=False)
    parts = jnp.transpose(parts, (1, 2, 0, 3, 4)).astype(jnp.float32)
    out_logits = (parts[:, :, :, 0] + parts[:, :, :, 1] + parts[:, :, :, 2]).reshape(-1)
    grad_msg, grad_self = grads[0], grads[1]
    return (out_logits, grad_msg, grad_self)


def solution(mesh):
    wide_devices, loop_devices = mesh.devices.shape
    split = Mesh(mesh.devices.reshape(wide_devices // 4, 2, 2, loop_devices), (*WIDE, "loop"))
    placed = (
        P("loop", None),
        P("loop", WIDE, None, None, None),
        P("loop", WIDE, None),
        P("loop", WIDE, None),
        P("loop", WIDE),
        P(),
        P(),
        P(),
        P("loop"),
    )
    return jax.shard_map(
        body, mesh=split, in_specs=placed, out_specs=(P("loop"), P(), P()), check_vma=False
    )
```

```python
import jax
import jax.numpy as jnp
from jax import lax
from jax.sharding import Mesh, PartitionSpec as P


def copy_for_each(value, axis):
    copies = jnp.broadcast_to(value, (lax.axis_size(axis), *value.shape))
    return lax.all_to_all(copies, axis, split_axis=0, concat_axis=0, tiled=True)


def laid_out(blocks, dim):
    shape = list(blocks.shape[1:])
    shape[dim] *= blocks.shape[0]
    return jnp.moveaxis(blocks, 0, dim).reshape(shape)


def gather_directly(value, axis, dim):
    blocks = copy_for_each(value, axis)
    return laid_out(blocks, dim)


def in_blocks(value, dim, devices):
    before, after = (value.shape[:dim], value.shape[dim + 1 :])
    return jnp.moveaxis(value.reshape(*before, devices, -1, *after), dim, 0)


def sum_at_owner(value, axis, dim):
    devices = lax.axis_size(axis)
    blocks = lax.all_to_all(in_blocks(value, dim, devices), axis, 0, 0, tiled=True)
    return jnp.sum(blocks.astype(jnp.float32), axis=0)


WIDE = ("wy", "wz", "wc")


def body(feats, tiles, tile_rows, tile_cols, tile_count, w_msg, w_self, readout, labels):
    rows_dev, feat_width = feats.shape
    size_tb = tiles.shape[-1]
    slot_count = tiles.shape[2]
    blocks_dev = rows_dev // size_tb
    wide_size = lax.axis_size(WIDE)
    cols_own = max(1, blocks_dev // wide_size)
    wide_pos = (lax.axis_index("wy") * lax.axis_size("wz") + lax.axis_index("wz")) * lax.axis_size(
        "wc"
    ) + lax.axis_index("wc")
    picked_blocks = wide_pos % blocks_dev + wide_size * jnp.arange(cols_own, dtype=jnp.int32)
    own_blocks = jnp.take(feats.reshape(blocks_dev, size_tb, feat_width), picked_blocks, axis=0)
    gathered = gather_directly(own_blocks, "loop", 0)
    tile_vals = tiles.reshape(slot_count, size_tb, size_tb)
    chosen = jnp.take(gathered, tile_cols.reshape(slot_count), axis=0)
    product = jnp.einsum("sij,sjd->sid", tile_vals, chosen, preferred_element_type=jnp.float32)
    valid_slot = jnp.arange(slot_count, dtype=jnp.int32) < tile_count.reshape(())
    placing = (
        (tile_rows.reshape(slot_count)[:, None] == jnp.arange(blocks_dev, dtype=jnp.int32)[None, :])
        & valid_slot[:, None]
    ).astype(jnp.float32)
    partial_value = jnp.einsum(
        "sr,sid->rid", placing, product, precision=lax.Precision.HIGHEST
    ).reshape(rows_dev, feat_width)
    core = lax.axis_index("wc")
    by_owner = partial_value.astype(jnp.bfloat16).reshape(
        lax.axis_size("wy"), lax.axis_size("wz"), lax.axis_size("wc"), -1, feat_width
    )
    keep = lax.dynamic_index_in_dim(by_owner, core, 2, keepdims=False)
    give = lax.dynamic_index_in_dim(by_owner, 1 - core, 2, keepdims=False)
    got = lax.ppermute(give, "wc", [(0, 1), (1, 0)])
    pair_sum = (keep.astype(jnp.float32) + got.astype(jnp.float32)).astype(jnp.bfloat16)
    pair_sum = pair_sum.reshape(-1, pair_sum.shape[-2], feat_width)
    message = sum_at_owner(pair_sum, ("wy", "wz"), 0).astype(jnp.bfloat16)
    message = message.reshape(-1, feat_width)
    share_rows = rows_dev // wide_size
    node_feats = lax.dynamic_slice_in_dim(feats, wide_pos * share_rows, share_rows, 0)
    node_labels = lax.dynamic_slice_in_dim(labels, wide_pos * share_rows, share_rows, 0)
    pre_act = jnp.dot(message, w_msg, preferred_element_type=jnp.float32) + jnp.dot(
        node_feats, w_self, preferred_element_type=jnp.float32
    )
    hidden = node_feats.astype(jnp.float32) + jax.nn.silu(pre_act)
    logits = jnp.dot(hidden, readout, precision=lax.Precision.HIGHEST)
    residual_grad = jax.nn.sigmoid(logits) - node_labels.astype(jnp.float32)
    gate_sig = jax.nn.sigmoid(pre_act)
    pre_grad = (
        residual_grad[:, None] * readout[None, :] * gate_sig * (1.0 + pre_act * (1.0 - gate_sig))
    ).astype(jnp.bfloat16)
    swap = [(0, 1), (1, 0)]
    others = ("wy", "wz", "loop")
    peers = lax.axis_size(others)
    sib_message, sib_pre_grad = lax.ppermute((message, pre_grad), "wc", swap)
    sib_feats = lax.dynamic_slice_in_dim(feats, (wide_pos + 1 - 2 * core) * share_rows, share_rows, 0)
    pair_rows = jnp.where(
        core == 0,
        jnp.concatenate([message, sib_message]),
        jnp.concatenate([node_feats, sib_feats]),
    )
    pair_grad = jnp.concatenate([pre_grad, sib_pre_grad])
    half_sum = jnp.einsum("na,nb->ab", pair_rows, pair_grad, preferred_element_type=jnp.float32)
    pieces = lax.all_to_all(half_sum.astype(jnp.bfloat16).reshape(peers, -1), others, 0, 0, tiled=True)
    reduced = jnp.sum(pieces.astype(jnp.float32), axis=0).astype(jnp.bfloat16)
    logit_hi = logits.astype(jnp.bfloat16)
    logit_rest = logits - logit_hi.astype(jnp.float32)
    logit_mid = logit_rest.astype(jnp.bfloat16)
    logit_lo = (logit_rest - logit_mid.astype(jnp.float32)).astype(jnp.bfloat16)
    payload = jnp.concatenate([reduced, logit_hi, logit_mid, logit_lo])
    gathered = lax.all_to_all(jnp.broadcast_to(payload, (peers, payload.size)), others, 0, 0, tiled=True)
    from_sibling = lax.ppermute(gathered, "wc", swap)
    by_core = jnp.where(core == 0, jnp.stack([gathered, from_sibling]), jnp.stack([from_sibling, gathered]))
    chunk = reduced.size
    grads = by_core[:, :, :chunk].reshape(2, feat_width, feat_width)
    parts = by_core[:, :, chunk:].reshape(
        2, lax.axis_size("wy"), lax.axis_size("wz"), lax.axis_size("loop"), 3, share_rows
    )
    parts = lax.dynamic_index_in_dim(parts, lax.axis_index("loop"), 3, keepdims=False)
    parts = jnp.transpose(parts, (1, 2, 0, 3, 4)).astype(jnp.float32)
    out_logits = (parts[:, :, :, 0] + parts[:, :, :, 1] + parts[:, :, :, 2]).reshape(-1)
    grad_msg, grad_self = grads[0], grads[1]
    return (out_logits, grad_msg, grad_self)


def solution(mesh):
    wide_devices, loop_devices = mesh.devices.shape
    split = Mesh(mesh.devices.reshape(wide_devices // 4, 2, 2, loop_devices), (*WIDE, "loop"))
    placed = (
        P("loop", None),
        P("loop", WIDE, None, None, None),
        P("loop", WIDE, None),
        P("loop", WIDE, None),
        P("loop", WIDE),
        P(),
        P(),
        P(),
        P("loop"),
    )
    return jax.shard_map(
        body, mesh=split, in_specs=placed, out_specs=(P("loop"), P(), P()), check_vma=False
    )
```

```python
import jax
import jax.numpy as jnp
from jax import lax
from jax.sharding import Mesh, PartitionSpec as P


def copy_for_each(value, axis):
    copies = jnp.broadcast_to(value, (lax.axis_size(axis), *value.shape))
    return lax.all_to_all(copies, axis, split_axis=0, concat_axis=0, tiled=True)


def laid_out(blocks, dim):
    shape = list(blocks.shape[1:])
    shape[dim] *= blocks.shape[0]
    return jnp.moveaxis(blocks, 0, dim).reshape(shape)


def gather_directly(value, axis, dim):
    blocks = copy_for_each(value, axis)
    return laid_out(blocks, dim)


def in_blocks(value, dim, devices):
    before, after = (value.shape[:dim], value.shape[dim + 1 :])
    return jnp.moveaxis(value.reshape(*before, devices, -1, *after), dim, 0)


def sum_at_owner(value, axis, dim):
    devices = lax.axis_size(axis)
    blocks = lax.all_to_all(in_blocks(value, dim, devices), axis, 0, 0, tiled=True)
    return jnp.sum(blocks.astype(jnp.float32), axis=0)


WIDE = ("wy", "wz", "wc")


def body(feats, tiles, tile_rows, tile_cols, tile_count, w_msg, w_self, readout, labels):
    rows_dev, feat_width = feats.shape
    size_tb = tiles.shape[-1]
    slot_count = tiles.shape[2]
    blocks_dev = rows_dev // size_tb
    wide_size = lax.axis_size(WIDE)
    cols_own = max(1, blocks_dev // wide_size)
    wide_pos = (lax.axis_index("wy") * lax.axis_size("wz") + lax.axis_index("wz")) * lax.axis_size(
        "wc"
    ) + lax.axis_index("wc")
    picked_blocks = wide_pos % blocks_dev + wide_size * jnp.arange(cols_own, dtype=jnp.int32)
    own_blocks = jnp.take(feats.reshape(blocks_dev, size_tb, feat_width), picked_blocks, axis=0)
    gathered = gather_directly(own_blocks, "loop", 0)
    tile_vals = tiles.reshape(slot_count, size_tb, size_tb)
    chosen = jnp.take(gathered, tile_cols.reshape(slot_count), axis=0)
    product = jnp.einsum("sij,sjd->sid", tile_vals, chosen, preferred_element_type=jnp.float32)
    valid_slot = jnp.arange(slot_count, dtype=jnp.int32) < tile_count.reshape(())
    placing = (
        (tile_rows.reshape(slot_count)[:, None] == jnp.arange(blocks_dev, dtype=jnp.int32)[None, :])
        & valid_slot[:, None]
    ).astype(jnp.float32)
    partial_value = jnp.einsum(
        "sr,sid->rid", placing, product, precision=lax.Precision.HIGHEST
    ).reshape(rows_dev, feat_width)
    core = lax.axis_index("wc")
    by_owner = partial_value.astype(jnp.bfloat16).reshape(
        lax.axis_size("wy"), lax.axis_size("wz"), lax.axis_size("wc"), -1, feat_width
    )
    keep = lax.dynamic_index_in_dim(by_owner, core, 2, keepdims=False)
    give = lax.dynamic_index_in_dim(by_owner, 1 - core, 2, keepdims=False)
    got = lax.ppermute(give, "wc", [(0, 1), (1, 0)])
    pair_sum = (keep.astype(jnp.float32) + got.astype(jnp.float32)).astype(jnp.bfloat16)
    pair_sum = pair_sum.reshape(-1, pair_sum.shape[-2], feat_width)
    message = sum_at_owner(pair_sum, ("wy", "wz"), 0).astype(jnp.bfloat16)
    message = message.reshape(-1, feat_width)
    share_rows = rows_dev // wide_size
    node_feats = lax.dynamic_slice_in_dim(feats, wide_pos * share_rows, share_rows, 0)
    node_labels = lax.dynamic_slice_in_dim(labels, wide_pos * share_rows, share_rows, 0)
    pre_act = jnp.dot(message, w_msg, preferred_element_type=jnp.float32) + jnp.dot(
        node_feats, w_self, preferred_element_type=jnp.float32
    )
    hidden = node_feats.astype(jnp.float32) + jax.nn.silu(pre_act)
    logits = jnp.dot(hidden, readout, precision=lax.Precision.HIGHEST)
    residual_grad = jax.nn.sigmoid(logits) - node_labels.astype(jnp.float32)
    gate_sig = jax.nn.sigmoid(pre_act)
    pre_grad = (
        residual_grad[:, None] * readout[None, :] * gate_sig * (1.0 + pre_act * (1.0 - gate_sig))
    ).astype(jnp.bfloat16)
    swap = [(0, 1), (1, 0)]
    others = ("wy", "wz", "loop")
    peers = lax.axis_size(others)
    sib_message, sib_pre_grad = lax.ppermute((message, pre_grad), "wc", swap)
    sib_feats = lax.dynamic_slice_in_dim(feats, (wide_pos + 1 - 2 * core) * share_rows, share_rows, 0)
    pair_rows = jnp.where(
        core == 0,
        jnp.concatenate([message, sib_message]),
        jnp.concatenate([node_feats, sib_feats]),
    )
    pair_grad = jnp.concatenate([pre_grad, sib_pre_grad])
    half_sum = jnp.einsum("na,nb->ab", pair_rows, pair_grad, preferred_element_type=jnp.float32)
    pieces = lax.all_to_all(
        half_sum.astype(jnp.bfloat16).reshape(peers, -1, feat_width), others, 0, 0, tiled=True
    )
    reduced = jnp.sum(pieces.astype(jnp.float32), axis=0).astype(jnp.bfloat16)
    logit_hi = logits.astype(jnp.bfloat16)
    logit_rest = logits - logit_hi.astype(jnp.float32)
    logit_mid = logit_rest.astype(jnp.bfloat16)
    logit_lo = (logit_rest - logit_mid.astype(jnp.float32)).astype(jnp.bfloat16)
    logit_parts = jnp.concatenate([logit_hi, logit_mid, logit_lo]).reshape(reduced.shape[0], -1)
    payload = jnp.concatenate([reduced, logit_parts], axis=1)
    gathered = lax.all_to_all(jnp.broadcast_to(payload, (peers, *payload.shape)), others, 0, 0, tiled=True)
    from_sibling = lax.ppermute(gathered, "wc", swap)
    by_core = jnp.where(core == 0, jnp.stack([gathered, from_sibling]), jnp.stack([from_sibling, gathered]))
    grads = by_core[:, :, :, :feat_width].reshape(2, feat_width, feat_width)
    parts = by_core[:, :, :, feat_width:].reshape(
        2, lax.axis_size("wy"), lax.axis_size("wz"), lax.axis_size("loop"), 3, share_rows
    )
    parts = lax.dynamic_index_in_dim(parts, lax.axis_index("loop"), 3, keepdims=False)
    parts = jnp.transpose(parts, (1, 2, 0, 3, 4)).astype(jnp.float32)
    out_logits = (parts[:, :, :, 0] + parts[:, :, :, 1] + parts[:, :, :, 2]).reshape(-1)
    grad_msg, grad_self = grads[0], grads[1]
    return (out_logits, grad_msg, grad_self)


def solution(mesh):
    wide_devices, loop_devices = mesh.devices.shape
    split = Mesh(mesh.devices.reshape(wide_devices // 4, 2, 2, loop_devices), (*WIDE, "loop"))
    placed = (
        P("loop", None),
        P("loop", WIDE, None, None, None),
        P("loop", WIDE, None),
        P("loop", WIDE, None),
        P("loop", WIDE),
        P(),
        P(),
        P(),
        P("loop"),
    )
    return jax.shard_map(
        body, mesh=split, in_specs=placed, out_specs=(P("loop"), P(), P()), check_vma=False
    )
```

```python
import jax
import jax.numpy as jnp
from jax import lax
from jax.sharding import Mesh, PartitionSpec as P


def copy_for_each(value, axis):
    copies = jnp.broadcast_to(value, (lax.axis_size(axis), *value.shape))
    return lax.all_to_all(copies, axis, split_axis=0, concat_axis=0, tiled=True)


def laid_out(blocks, dim):
    shape = list(blocks.shape[1:])
    shape[dim] *= blocks.shape[0]
    return jnp.moveaxis(blocks, 0, dim).reshape(shape)


def gather_directly(value, axis, dim):
    blocks = copy_for_each(value, axis)
    return laid_out(blocks, dim)


def in_blocks(value, dim, devices):
    before, after = (value.shape[:dim], value.shape[dim + 1 :])
    return jnp.moveaxis(value.reshape(*before, devices, -1, *after), dim, 0)


def sum_at_owner(value, axis, dim):
    devices = lax.axis_size(axis)
    blocks = lax.all_to_all(in_blocks(value, dim, devices), axis, 0, 0, tiled=True)
    return jnp.sum(blocks.astype(jnp.float32), axis=0)


WIDE = ("wy", "wz", "wc")


def body(feats, tiles, tile_rows, tile_cols, tile_count, w_msg, w_self, readout, labels):
    rows_dev, feat_width = feats.shape
    size_tb = tiles.shape[-1]
    slot_count = tiles.shape[2]
    blocks_dev = rows_dev // size_tb
    wide_size = lax.axis_size(WIDE)
    cols_own = max(1, blocks_dev // wide_size)
    wide_pos = (lax.axis_index("wy") * lax.axis_size("wz") + lax.axis_index("wz")) * lax.axis_size(
        "wc"
    ) + lax.axis_index("wc")
    picked_blocks = wide_pos % blocks_dev + wide_size * jnp.arange(cols_own, dtype=jnp.int32)
    own_blocks = jnp.take(feats.reshape(blocks_dev, size_tb, feat_width), picked_blocks, axis=0)
    gathered = gather_directly(own_blocks, "loop", 0)
    tile_vals = tiles.reshape(slot_count, size_tb, size_tb)
    chosen = jnp.take(gathered, tile_cols.reshape(slot_count), axis=0)
    product = jnp.einsum("sij,sjd->sid", tile_vals, chosen, preferred_element_type=jnp.float32)
    valid_slot = jnp.arange(slot_count, dtype=jnp.int32) < tile_count.reshape(())
    placing = (
        (tile_rows.reshape(slot_count)[:, None] == jnp.arange(blocks_dev, dtype=jnp.int32)[None, :])
        & valid_slot[:, None]
    ).astype(jnp.float32)
    partial_value = jnp.einsum(
        "sr,sid->rid", placing, product, precision=lax.Precision.HIGHEST
    ).reshape(rows_dev, feat_width)
    core = lax.axis_index("wc")
    by_owner = partial_value.astype(jnp.bfloat16).reshape(
        lax.axis_size("wy"), lax.axis_size("wz"), lax.axis_size("wc"), -1, feat_width
    )
    keep = lax.dynamic_index_in_dim(by_owner, core, 2, keepdims=False)
    give = lax.dynamic_index_in_dim(by_owner, 1 - core, 2, keepdims=False)
    got = lax.ppermute(give, "wc", [(0, 1), (1, 0)])
    pair_sum = (keep.astype(jnp.float32) + got.astype(jnp.float32)).astype(jnp.bfloat16)
    pair_sum = pair_sum.reshape(-1, pair_sum.shape[-2], feat_width)
    message = sum_at_owner(pair_sum, ("wy", "wz"), 0).astype(jnp.bfloat16)
    message = message.reshape(-1, feat_width)
    share_rows = rows_dev // wide_size
    node_feats = lax.dynamic_slice_in_dim(feats, wide_pos * share_rows, share_rows, 0)
    node_labels = lax.dynamic_slice_in_dim(labels, wide_pos * share_rows, share_rows, 0)
    pre_act = jnp.dot(message, w_msg, preferred_element_type=jnp.float32) + jnp.dot(
        node_feats, w_self, preferred_element_type=jnp.float32
    )
    hidden = node_feats.astype(jnp.float32) + jax.nn.silu(pre_act)
    logits = jnp.dot(hidden, readout, precision=lax.Precision.HIGHEST)
    residual_grad = jax.nn.sigmoid(logits) - node_labels.astype(jnp.float32)
    gate_sig = jax.nn.sigmoid(pre_act)
    pre_grad = (
        residual_grad[:, None] * readout[None, :] * gate_sig * (1.0 + pre_act * (1.0 - gate_sig))
    ).astype(jnp.bfloat16)
    swap = [(0, 1), (1, 0)]
    others = ("wy", "wz", "loop")
    peers = lax.axis_size(others)
    sib_message, sib_pre_grad = lax.ppermute((message, pre_grad), "wc", swap)
    sib_feats = lax.dynamic_slice_in_dim(feats, (wide_pos + 1 - 2 * core) * share_rows, share_rows, 0)
    pair_rows = jnp.where(
        core == 0,
        jnp.concatenate([message, sib_message]),
        jnp.concatenate([node_feats, sib_feats]),
    )
    pair_grad = jnp.concatenate([pre_grad, sib_pre_grad])
    half_sum = jnp.einsum("na,nb->ab", pair_rows, pair_grad, preferred_element_type=jnp.float32)
    pieces = lax.all_to_all(
        half_sum.astype(jnp.bfloat16).reshape(peers, -1, feat_width), others, 0, 0, tiled=True
    )
    reduced = jnp.sum(pieces.astype(jnp.float32), axis=0).astype(jnp.bfloat16)
    logit_hi = logits.astype(jnp.bfloat16)
    logit_rest = logits - logit_hi.astype(jnp.float32)
    logit_mid = logit_rest.astype(jnp.bfloat16)
    logit_lo = (logit_rest - logit_mid.astype(jnp.float32)).astype(jnp.bfloat16)
    logit_parts = jnp.concatenate([logit_hi, logit_mid, logit_lo]).reshape(reduced.shape[0], -1)
    payload = jnp.concatenate([reduced, logit_parts], axis=1)
    gathered = lax.all_to_all(jnp.broadcast_to(payload, (peers, *payload.shape)), others, 0, 0, tiled=True)
    from_sibling = lax.ppermute(gathered, "wc", swap)
    from_core0 = jnp.where(core == 0, gathered, from_sibling)
    from_core1 = jnp.where(core == 0, from_sibling, gathered)
    grad_msg = from_core0[:, :, :feat_width].reshape(feat_width, feat_width)
    grad_self = from_core1[:, :, :feat_width].reshape(feat_width, feat_width)
    by_core = jnp.stack([from_core0[:, :, feat_width:], from_core1[:, :, feat_width:]])
    parts = by_core.reshape(
        2, lax.axis_size("wy"), lax.axis_size("wz"), lax.axis_size("loop"), 3, share_rows
    )
    parts = lax.dynamic_index_in_dim(parts, lax.axis_index("loop"), 3, keepdims=False)
    parts = jnp.transpose(parts, (1, 2, 0, 3, 4)).astype(jnp.float32)
    out_logits = (parts[:, :, :, 0] + parts[:, :, :, 1] + parts[:, :, :, 2]).reshape(-1)
    return (out_logits, grad_msg, grad_self)


def solution(mesh):
    wide_devices, loop_devices = mesh.devices.shape
    split = Mesh(mesh.devices.reshape(wide_devices // 4, 2, 2, loop_devices), (*WIDE, "loop"))
    placed = (
        P("loop", None),
        P("loop", WIDE, None, None, None),
        P("loop", WIDE, None),
        P("loop", WIDE, None),
        P("loop", WIDE),
        P(),
        P(),
        P(),
        P("loop"),
    )
    return jax.shard_map(
        body, mesh=split, in_specs=placed, out_specs=(P("loop"), P(), P()), check_vma=False
    )
```

```python
import jax
import jax.numpy as jnp
from jax import lax
from jax.sharding import Mesh, PartitionSpec as P


def copy_for_each(value, axis):
    copies = jnp.broadcast_to(value, (lax.axis_size(axis), *value.shape))
    return lax.all_to_all(copies, axis, split_axis=0, concat_axis=0, tiled=True)


def laid_out(blocks, dim):
    shape = list(blocks.shape[1:])
    shape[dim] *= blocks.shape[0]
    return jnp.moveaxis(blocks, 0, dim).reshape(shape)


def gather_directly(value, axis, dim):
    blocks = copy_for_each(value, axis)
    return laid_out(blocks, dim)


def in_blocks(value, dim, devices):
    before, after = (value.shape[:dim], value.shape[dim + 1 :])
    return jnp.moveaxis(value.reshape(*before, devices, -1, *after), dim, 0)


def sum_at_owner(value, axis, dim):
    devices = lax.axis_size(axis)
    blocks = lax.all_to_all(in_blocks(value, dim, devices), axis, 0, 0, tiled=True)
    return jnp.sum(blocks.astype(jnp.float32), axis=0)


WIDE = ("wy", "wz", "wc")


def body(feats, tiles, tile_rows, tile_cols, tile_count, w_msg, w_self, readout, labels):
    rows_dev, feat_width = feats.shape
    size_tb = tiles.shape[-1]
    slot_count = tiles.shape[2]
    blocks_dev = rows_dev // size_tb
    wide_size = lax.axis_size(WIDE)
    cols_own = max(1, blocks_dev // wide_size)
    wide_pos = (lax.axis_index("wy") * lax.axis_size("wz") + lax.axis_index("wz")) * lax.axis_size(
        "wc"
    ) + lax.axis_index("wc")
    picked_blocks = wide_pos % blocks_dev + wide_size * jnp.arange(cols_own, dtype=jnp.int32)
    own_blocks = jnp.take(feats.reshape(blocks_dev, size_tb, feat_width), picked_blocks, axis=0)
    gathered = gather_directly(own_blocks, "loop", 0)
    tile_vals = tiles.reshape(slot_count, size_tb, size_tb)
    chosen = jnp.take(gathered, tile_cols.reshape(slot_count), axis=0)
    product = jnp.einsum("sij,sjd->sid", tile_vals, chosen, preferred_element_type=jnp.float32)
    valid_slot = jnp.arange(slot_count, dtype=jnp.int32) < tile_count.reshape(())
    placing = (
        (tile_rows.reshape(slot_count)[:, None] == jnp.arange(blocks_dev, dtype=jnp.int32)[None, :])
        & valid_slot[:, None]
    ).astype(jnp.float32)
    partial_value = jnp.einsum(
        "sr,sid->rid", placing, product, precision=lax.Precision.HIGHEST
    ).reshape(rows_dev, feat_width)
    core = lax.axis_index("wc")
    by_owner = partial_value.astype(jnp.bfloat16).reshape(
        lax.axis_size("wy"), lax.axis_size("wz"), lax.axis_size("wc"), -1, feat_width
    )
    keep = lax.dynamic_index_in_dim(by_owner, core, 2, keepdims=False)
    give = lax.dynamic_index_in_dim(by_owner, 1 - core, 2, keepdims=False)
    got = lax.ppermute(give, "wc", [(0, 1), (1, 0)])
    pair_sum = (keep.astype(jnp.float32) + got.astype(jnp.float32)).astype(jnp.bfloat16)
    pair_sum = pair_sum.reshape(-1, pair_sum.shape[-2], feat_width)
    message = sum_at_owner(pair_sum, ("wy", "wz"), 0).astype(jnp.bfloat16)
    message = message.reshape(-1, feat_width)
    share_rows = rows_dev // wide_size
    node_feats = lax.dynamic_slice_in_dim(feats, wide_pos * share_rows, share_rows, 0)
    node_labels = lax.dynamic_slice_in_dim(labels, wide_pos * share_rows, share_rows, 0)
    pre_act = jnp.dot(message, w_msg, preferred_element_type=jnp.float32) + jnp.dot(
        node_feats, w_self, preferred_element_type=jnp.float32
    )
    hidden = node_feats.astype(jnp.float32) + jax.nn.silu(pre_act)
    logits = jnp.dot(hidden, readout, precision=lax.Precision.HIGHEST)
    residual_grad = jax.nn.sigmoid(logits) - node_labels.astype(jnp.float32)
    gate_sig = jax.nn.sigmoid(pre_act)
    pre_grad = (
        residual_grad[:, None] * readout[None, :] * gate_sig * (1.0 + pre_act * (1.0 - gate_sig))
    ).astype(jnp.bfloat16)
    swap = [(0, 1), (1, 0)]
    others = ("wy", "wz", "loop")
    peers = lax.axis_size(others)
    sib_message, sib_pre_grad = lax.ppermute((message, pre_grad), "wc", swap)
    sib_feats = lax.dynamic_slice_in_dim(feats, (wide_pos + 1 - 2 * core) * share_rows, share_rows, 0)
    pair_rows = jnp.where(
        core == 0,
        jnp.concatenate([message, sib_message]),
        jnp.concatenate([node_feats, sib_feats]),
    )
    pair_grad = jnp.concatenate([pre_grad, sib_pre_grad])
    half_sum = jnp.einsum("na,nb->ab", pair_rows, pair_grad, preferred_element_type=jnp.float32)
    pieces = lax.all_to_all(
        half_sum.astype(jnp.bfloat16).reshape(peers, -1, feat_width), others, 0, 0, tiled=True
    )
    reduced = jnp.sum(pieces.astype(jnp.float32), axis=0).astype(jnp.bfloat16)
    logit_hi = logits.astype(jnp.bfloat16)
    logit_rest = logits - logit_hi.astype(jnp.float32)
    logit_mid = logit_rest.astype(jnp.bfloat16)
    logit_lo = (logit_rest - logit_mid.astype(jnp.float32)).astype(jnp.bfloat16)
    logit_parts = jnp.concatenate([logit_hi, logit_mid, logit_lo]).reshape(reduced.shape[0], -1)
    payload = jnp.concatenate([reduced, logit_parts], axis=1)
    gathered = lax.all_to_all(jnp.tile(payload, (peers, 1)), others, 0, 0, tiled=True)
    from_sibling = lax.ppermute(gathered, "wc", swap)
    from_core0 = jnp.where(core == 0, gathered, from_sibling)
    from_core1 = jnp.where(core == 0, from_sibling, gathered)
    grad_msg = from_core0[:, :feat_width]
    grad_self = from_core1[:, :feat_width]
    by_core = jnp.stack([from_core0[:, feat_width:], from_core1[:, feat_width:]])
    parts = by_core.reshape(
        2, lax.axis_size("wy"), lax.axis_size("wz"), lax.axis_size("loop"), 3, share_rows
    )
    parts = lax.dynamic_index_in_dim(parts, lax.axis_index("loop"), 3, keepdims=False)
    parts = jnp.transpose(parts, (1, 2, 0, 3, 4)).astype(jnp.float32)
    out_logits = (parts[:, :, :, 0] + parts[:, :, :, 1] + parts[:, :, :, 2]).reshape(-1)
    return (out_logits, grad_msg, grad_self)


def solution(mesh):
    wide_devices, loop_devices = mesh.devices.shape
    split = Mesh(mesh.devices.reshape(wide_devices // 4, 2, 2, loop_devices), (*WIDE, "loop"))
    placed = (
        P("loop", None),
        P("loop", WIDE, None, None, None),
        P("loop", WIDE, None),
        P("loop", WIDE, None),
        P("loop", WIDE),
        P(),
        P(),
        P(),
        P("loop"),
    )
    return jax.shard_map(
        body, mesh=split, in_specs=placed, out_specs=(P("loop"), P(), P()), check_vma=False
    )
```

```python
import jax
import jax.numpy as jnp
from jax import lax
from jax.sharding import Mesh, PartitionSpec as P


def copy_for_each(value, axis):
    copies = jnp.broadcast_to(value, (lax.axis_size(axis), *value.shape))
    return lax.all_to_all(copies, axis, split_axis=0, concat_axis=0, tiled=True)


def laid_out(blocks, dim):
    shape = list(blocks.shape[1:])
    shape[dim] *= blocks.shape[0]
    return jnp.moveaxis(blocks, 0, dim).reshape(shape)


def gather_directly(value, axis, dim):
    blocks = copy_for_each(value, axis)
    return laid_out(blocks, dim)


def in_blocks(value, dim, devices):
    before, after = (value.shape[:dim], value.shape[dim + 1 :])
    return jnp.moveaxis(value.reshape(*before, devices, -1, *after), dim, 0)


def sum_at_owner(value, axis, dim):
    devices = lax.axis_size(axis)
    blocks = lax.all_to_all(in_blocks(value, dim, devices), axis, 0, 0, tiled=True)
    return jnp.sum(blocks.astype(jnp.float32), axis=0)


WIDE = ("wy", "wz", "wc")


def body(feats, tiles, tile_rows, tile_cols, tile_count, w_msg, w_self, readout, labels):
    rows_dev, feat_width = feats.shape
    size_tb = tiles.shape[-1]
    slot_count = tiles.shape[2]
    blocks_dev = rows_dev // size_tb
    wide_size = lax.axis_size(WIDE)
    cols_own = max(1, blocks_dev // wide_size)
    wide_pos = (lax.axis_index("wy") * lax.axis_size("wz") + lax.axis_index("wz")) * lax.axis_size(
        "wc"
    ) + lax.axis_index("wc")
    picked_blocks = wide_pos % blocks_dev + wide_size * jnp.arange(cols_own, dtype=jnp.int32)
    own_blocks = jnp.take(feats.reshape(blocks_dev, size_tb, feat_width), picked_blocks, axis=0)
    gathered = gather_directly(own_blocks, "loop", 0)
    tile_vals = tiles.reshape(slot_count, size_tb, size_tb)
    chosen = jnp.take(gathered, tile_cols.reshape(slot_count), axis=0)
    product = jnp.einsum("sij,sjd->sid", tile_vals, chosen, preferred_element_type=jnp.float32)
    valid_slot = jnp.arange(slot_count, dtype=jnp.int32) < tile_count.reshape(())
    placing = (
        (tile_rows.reshape(slot_count)[:, None] == jnp.arange(blocks_dev, dtype=jnp.int32)[None, :])
        & valid_slot[:, None]
    ).astype(jnp.float32)
    partial_value = jnp.einsum(
        "sr,sid->rid", placing, product, precision=lax.Precision.HIGHEST
    ).reshape(rows_dev, feat_width)
    core = lax.axis_index("wc")
    by_owner = partial_value.astype(jnp.bfloat16).reshape(
        lax.axis_size("wy"), lax.axis_size("wz"), lax.axis_size("wc"), -1, feat_width
    )
    keep = lax.dynamic_index_in_dim(by_owner, core, 2, keepdims=False)
    give = lax.dynamic_index_in_dim(by_owner, 1 - core, 2, keepdims=False)
    got = lax.ppermute(give, "wc", [(0, 1), (1, 0)])
    pair_sum = (keep.astype(jnp.float32) + got.astype(jnp.float32)).astype(jnp.bfloat16)
    pair_sum = pair_sum.reshape(-1, pair_sum.shape[-2], feat_width)
    message = sum_at_owner(pair_sum, ("wy", "wz"), 0).astype(jnp.bfloat16)
    message = message.reshape(-1, feat_width)
    share_rows = rows_dev // wide_size
    node_feats = lax.dynamic_slice_in_dim(feats, wide_pos * share_rows, share_rows, 0)
    node_labels = lax.dynamic_slice_in_dim(labels, wide_pos * share_rows, share_rows, 0)
    pre_act = jnp.dot(message, w_msg, preferred_element_type=jnp.float32) + jnp.dot(
        node_feats, w_self, preferred_element_type=jnp.float32
    )
    hidden = node_feats.astype(jnp.float32) + jax.nn.silu(pre_act)
    logits = jnp.dot(hidden, readout, precision=lax.Precision.HIGHEST)
    residual_grad = jax.nn.sigmoid(logits) - node_labels.astype(jnp.float32)
    gate_sig = jax.nn.sigmoid(pre_act)
    pre_grad = (
        residual_grad[:, None] * readout[None, :] * gate_sig * (1.0 + pre_act * (1.0 - gate_sig))
    ).astype(jnp.bfloat16)
    swap = [(0, 1), (1, 0)]
    others = ("wy", "wz", "loop")
    peers = lax.axis_size(others)
    sib_message, sib_pre_grad = lax.ppermute((message, pre_grad), "wc", swap)
    sib_feats = lax.dynamic_slice_in_dim(feats, (wide_pos + 1 - 2 * core) * share_rows, share_rows, 0)
    pair_rows = jnp.where(
        core == 0,
        jnp.concatenate([message, sib_message]),
        jnp.concatenate([node_feats, sib_feats]),
    )
    pair_grad = jnp.concatenate([pre_grad, sib_pre_grad])
    half_sum = jnp.einsum("na,nb->ab", pair_rows, pair_grad, preferred_element_type=jnp.float32)
    pieces = lax.all_to_all(half_sum.astype(jnp.bfloat16), others, 0, 0, tiled=True)
    reduced = jnp.sum(pieces.reshape(peers, -1, feat_width).astype(jnp.float32), axis=0)
    reduced = reduced.astype(jnp.bfloat16)
    logit_hi = logits.astype(jnp.bfloat16)
    logit_rest = logits - logit_hi.astype(jnp.float32)
    logit_mid = logit_rest.astype(jnp.bfloat16)
    logit_lo = (logit_rest - logit_mid.astype(jnp.float32)).astype(jnp.bfloat16)
    logit_parts = jnp.concatenate([logit_hi, logit_mid, logit_lo]).reshape(reduced.shape[0], -1)
    payload = jnp.concatenate([reduced, logit_parts], axis=1)
    gathered = lax.all_to_all(jnp.tile(payload, (peers, 1)), others, 0, 0, tiled=True)
    from_sibling = lax.ppermute(gathered, "wc", swap)
    from_core0 = jnp.where(core == 0, gathered, from_sibling)
    from_core1 = jnp.where(core == 0, from_sibling, gathered)
    grad_msg = from_core0[:, :feat_width]
    grad_self = from_core1[:, :feat_width]
    by_core = jnp.stack([from_core0[:, feat_width:], from_core1[:, feat_width:]])
    parts = by_core.reshape(
        2, lax.axis_size("wy"), lax.axis_size("wz"), lax.axis_size("loop"), 3, share_rows
    )
    parts = lax.dynamic_index_in_dim(parts, lax.axis_index("loop"), 3, keepdims=False)
    parts = jnp.transpose(parts, (1, 2, 0, 3, 4)).astype(jnp.float32)
    out_logits = (parts[:, :, :, 0] + parts[:, :, :, 1] + parts[:, :, :, 2]).reshape(-1)
    return (out_logits, grad_msg, grad_self)


def solution(mesh):
    wide_devices, loop_devices = mesh.devices.shape
    split = Mesh(mesh.devices.reshape(wide_devices // 4, 2, 2, loop_devices), (*WIDE, "loop"))
    placed = (
        P("loop", None),
        P("loop", WIDE, None, None, None),
        P("loop", WIDE, None),
        P("loop", WIDE, None),
        P("loop", WIDE),
        P(),
        P(),
        P(),
        P("loop"),
    )
    return jax.shard_map(
        body, mesh=split, in_specs=placed, out_specs=(P("loop"), P(), P()), check_vma=False
    )
```

```python
import jax
import jax.numpy as jnp
from jax import lax
from jax.sharding import Mesh, PartitionSpec as P


def copy_for_each(value, axis):
    copies = jnp.broadcast_to(value, (lax.axis_size(axis), *value.shape))
    return lax.all_to_all(copies, axis, split_axis=0, concat_axis=0, tiled=True)


def laid_out(blocks, dim):
    shape = list(blocks.shape[1:])
    shape[dim] *= blocks.shape[0]
    return jnp.moveaxis(blocks, 0, dim).reshape(shape)


def gather_directly(value, axis, dim):
    blocks = copy_for_each(value, axis)
    return laid_out(blocks, dim)


def in_blocks(value, dim, devices):
    before, after = (value.shape[:dim], value.shape[dim + 1 :])
    return jnp.moveaxis(value.reshape(*before, devices, -1, *after), dim, 0)


def sum_at_owner(value, axis, dim):
    devices = lax.axis_size(axis)
    blocks = lax.all_to_all(in_blocks(value, dim, devices), axis, 0, 0, tiled=True)
    return jnp.sum(blocks.astype(jnp.float32), axis=0)


WIDE = ("wy", "wz", "wc")


def body(feats, tiles, tile_rows, tile_cols, tile_count, w_msg, w_self, readout, labels):
    rows_dev, feat_width = feats.shape
    size_tb = tiles.shape[-1]
    slot_count = tiles.shape[2]
    blocks_dev = rows_dev // size_tb
    wide_size = lax.axis_size(WIDE)
    cols_own = max(1, blocks_dev // wide_size)
    wide_pos = (lax.axis_index("wy") * lax.axis_size("wz") + lax.axis_index("wz")) * lax.axis_size(
        "wc"
    ) + lax.axis_index("wc")
    picked_blocks = wide_pos % blocks_dev + wide_size * jnp.arange(cols_own, dtype=jnp.int32)
    if cols_own == 1:
        own_blocks = lax.dynamic_slice_in_dim(feats, picked_blocks[0] * size_tb, size_tb, 0)[None]
    else:
        own_blocks = jnp.take(feats.reshape(blocks_dev, size_tb, feat_width), picked_blocks, axis=0)
    gathered = gather_directly(own_blocks, "loop", 0)
    tile_vals = tiles.reshape(slot_count, size_tb, size_tb)
    chosen = jnp.take(gathered, tile_cols.reshape(slot_count), axis=0)
    product = jnp.einsum("sij,sjd->sid", tile_vals, chosen, preferred_element_type=jnp.float32)
    valid_slot = jnp.arange(slot_count, dtype=jnp.int32) < tile_count.reshape(())
    placing = (
        (tile_rows.reshape(slot_count)[:, None] == jnp.arange(blocks_dev, dtype=jnp.int32)[None, :])
        & valid_slot[:, None]
    ).astype(jnp.float32)
    partial_value = jnp.einsum(
        "sr,sid->rid", placing, product, precision=lax.Precision.HIGHEST
    ).reshape(rows_dev, feat_width)
    core = lax.axis_index("wc")
    by_owner = partial_value.astype(jnp.bfloat16).reshape(
        lax.axis_size("wy"), lax.axis_size("wz"), lax.axis_size("wc"), -1, feat_width
    )
    keep = lax.dynamic_index_in_dim(by_owner, core, 2, keepdims=False)
    give = lax.dynamic_index_in_dim(by_owner, 1 - core, 2, keepdims=False)
    got = lax.ppermute(give, "wc", [(0, 1), (1, 0)])
    pair_sum = (keep.astype(jnp.float32) + got.astype(jnp.float32)).astype(jnp.bfloat16)
    pair_sum = pair_sum.reshape(-1, pair_sum.shape[-2], feat_width)
    message = sum_at_owner(pair_sum, ("wy", "wz"), 0).astype(jnp.bfloat16)
    message = message.reshape(-1, feat_width)
    share_rows = rows_dev // wide_size
    node_feats = lax.dynamic_slice_in_dim(feats, wide_pos * share_rows, share_rows, 0)
    node_labels = lax.dynamic_slice_in_dim(labels, wide_pos * share_rows, share_rows, 0)
    pre_act = jnp.dot(message, w_msg, preferred_element_type=jnp.float32) + jnp.dot(
        node_feats, w_self, preferred_element_type=jnp.float32
    )
    hidden = node_feats.astype(jnp.float32) + jax.nn.silu(pre_act)
    logits = jnp.dot(hidden, readout, precision=lax.Precision.HIGHEST)
    residual_grad = jax.nn.sigmoid(logits) - node_labels.astype(jnp.float32)
    gate_sig = jax.nn.sigmoid(pre_act)
    pre_grad = (
        residual_grad[:, None] * readout[None, :] * gate_sig * (1.0 + pre_act * (1.0 - gate_sig))
    ).astype(jnp.bfloat16)
    swap = [(0, 1), (1, 0)]
    others = ("wy", "wz", "loop")
    peers = lax.axis_size(others)
    sib_message, sib_pre_grad = lax.ppermute((message, pre_grad), "wc", swap)
    sib_feats = lax.dynamic_slice_in_dim(feats, (wide_pos + 1 - 2 * core) * share_rows, share_rows, 0)
    pair_rows = jnp.where(
        core == 0,
        jnp.concatenate([message, sib_message]),
        jnp.concatenate([node_feats, sib_feats]),
    )
    pair_grad = jnp.concatenate([pre_grad, sib_pre_grad])
    half_sum = jnp.einsum("na,nb->ab", pair_rows, pair_grad, preferred_element_type=jnp.float32)
    pieces = lax.all_to_all(
        half_sum.astype(jnp.bfloat16).reshape(peers, -1, feat_width), others, 0, 0, tiled=True
    )
    reduced = jnp.sum(pieces.astype(jnp.float32), axis=0).astype(jnp.bfloat16)
    logit_hi = logits.astype(jnp.bfloat16)
    logit_rest = logits - logit_hi.astype(jnp.float32)
    logit_mid = logit_rest.astype(jnp.bfloat16)
    logit_lo = (logit_rest - logit_mid.astype(jnp.float32)).astype(jnp.bfloat16)
    logit_parts = jnp.concatenate([logit_hi, logit_mid, logit_lo]).reshape(reduced.shape[0], -1)
    payload = jnp.concatenate([reduced, logit_parts], axis=1)
    gathered = lax.all_to_all(jnp.tile(payload, (peers, 1)), others, 0, 0, tiled=True)
    from_sibling = lax.ppermute(gathered, "wc", swap)
    from_core0 = jnp.where(core == 0, gathered, from_sibling)
    from_core1 = jnp.where(core == 0, from_sibling, gathered)
    grad_msg = from_core0[:, :feat_width]
    grad_self = from_core1[:, :feat_width]
    by_core = jnp.stack([from_core0[:, feat_width:], from_core1[:, feat_width:]])
    parts = by_core.reshape(
        2, lax.axis_size("wy"), lax.axis_size("wz"), lax.axis_size("loop"), 3, share_rows
    )
    parts = lax.dynamic_index_in_dim(parts, lax.axis_index("loop"), 3, keepdims=False)
    parts = jnp.transpose(parts, (1, 2, 0, 3, 4)).astype(jnp.float32)
    out_logits = (parts[:, :, :, 0] + parts[:, :, :, 1] + parts[:, :, :, 2]).reshape(-1)
    return (out_logits, grad_msg, grad_self)


def solution(mesh):
    wide_devices, loop_devices = mesh.devices.shape
    split = Mesh(mesh.devices.reshape(wide_devices // 4, 2, 2, loop_devices), (*WIDE, "loop"))
    placed = (
        P("loop", None),
        P("loop", WIDE, None, None, None),
        P("loop", WIDE, None),
        P("loop", WIDE, None),
        P("loop", WIDE),
        P(),
        P(),
        P(),
        P("loop"),
    )
    return jax.shard_map(
        body, mesh=split, in_specs=placed, out_specs=(P("loop"), P(), P()), check_vma=False
    )
```

```python
import jax
import jax.numpy as jnp
from jax import lax
from jax.sharding import Mesh, PartitionSpec as P


def copy_for_each(value, axis):
    copies = jnp.broadcast_to(value, (lax.axis_size(axis), *value.shape))
    return lax.all_to_all(copies, axis, split_axis=0, concat_axis=0, tiled=True)


def laid_out(blocks, dim):
    shape = list(blocks.shape[1:])
    shape[dim] *= blocks.shape[0]
    return jnp.moveaxis(blocks, 0, dim).reshape(shape)


def gather_directly(value, axis, dim):
    blocks = copy_for_each(value, axis)
    return laid_out(blocks, dim)


def in_blocks(value, dim, devices):
    before, after = (value.shape[:dim], value.shape[dim + 1 :])
    return jnp.moveaxis(value.reshape(*before, devices, -1, *after), dim, 0)


def sum_at_owner(value, axis, dim):
    devices = lax.axis_size(axis)
    blocks = lax.all_to_all(in_blocks(value, dim, devices), axis, 0, 0, tiled=True)
    return jnp.sum(blocks.astype(jnp.float32), axis=0)


WIDE = ("wy", "wz", "wc")


def body(feats, tiles, tile_rows, tile_cols, tile_count, w_msg, w_self, readout, labels):
    rows_dev, feat_width = feats.shape
    size_tb = tiles.shape[-1]
    slot_count = tiles.shape[2]
    blocks_dev = rows_dev // size_tb
    wide_size = lax.axis_size(WIDE)
    cols_own = max(1, blocks_dev // wide_size)
    wide_pos = (lax.axis_index("wy") * lax.axis_size("wz") + lax.axis_index("wz")) * lax.axis_size(
        "wc"
    ) + lax.axis_index("wc")
    picked_blocks = wide_pos % blocks_dev + wide_size * jnp.arange(cols_own, dtype=jnp.int32)
    if cols_own == 1:
        own_blocks = lax.dynamic_slice_in_dim(feats, picked_blocks[0] * size_tb, size_tb, 0)[None]
    else:
        own_blocks = jnp.take(feats.reshape(blocks_dev, size_tb, feat_width), picked_blocks, axis=0)
    gathered = gather_directly(own_blocks, "loop", 0)
    tile_vals = tiles.reshape(slot_count, size_tb, size_tb)
    chosen = jnp.take(gathered, tile_cols.reshape(slot_count), axis=0)
    product = jnp.einsum("sij,sjd->sid", tile_vals, chosen, preferred_element_type=jnp.float32)
    valid_slot = jnp.arange(slot_count, dtype=jnp.int32) < tile_count.reshape(())
    placing = (
        (tile_rows.reshape(slot_count)[:, None] == jnp.arange(blocks_dev, dtype=jnp.int32)[None, :])
        & valid_slot[:, None]
    ).astype(jnp.float32)
    partial_value = jnp.einsum(
        "sr,sid->rid", placing, product, precision=lax.Precision.HIGHEST
    ).reshape(rows_dev, feat_width)
    core = lax.axis_index("wc")
    by_owner = partial_value.astype(jnp.bfloat16).reshape(
        lax.axis_size("wy"), lax.axis_size("wz"), lax.axis_size("wc"), -1, feat_width
    )
    keep = lax.dynamic_index_in_dim(by_owner, core, 2, keepdims=False)
    give = lax.dynamic_index_in_dim(by_owner, 1 - core, 2, keepdims=False)
    got = lax.ppermute(give, "wc", [(0, 1), (1, 0)])
    pair_sum = (keep.astype(jnp.float32) + got.astype(jnp.float32)).astype(jnp.bfloat16)
    pair_sum = pair_sum.reshape(-1, pair_sum.shape[-2], feat_width)
    message = sum_at_owner(pair_sum, ("wy", "wz"), 0).astype(jnp.bfloat16)
    message = message.reshape(-1, feat_width)
    share_rows = rows_dev // wide_size
    node_feats = lax.dynamic_slice_in_dim(feats, wide_pos * share_rows, share_rows, 0)
    node_labels = lax.dynamic_slice_in_dim(labels, wide_pos * share_rows, share_rows, 0)
    pre_act = jnp.dot(message, w_msg, preferred_element_type=jnp.float32) + jnp.dot(
        node_feats, w_self, preferred_element_type=jnp.float32
    )
    hidden = node_feats.astype(jnp.float32) + jax.nn.silu(pre_act)
    logits = jnp.dot(hidden, readout, precision=lax.Precision.HIGHEST)
    residual_grad = jax.nn.sigmoid(logits) - node_labels.astype(jnp.float32)
    gate_sig = jax.nn.sigmoid(pre_act)
    pre_grad = (
        residual_grad[:, None] * readout[None, :] * gate_sig * (1.0 + pre_act * (1.0 - gate_sig))
    ).astype(jnp.bfloat16)
    swap = [(0, 1), (1, 0)]
    others = ("wy", "wz", "loop")
    peers = lax.axis_size(others)
    sib_message, sib_pre_grad = lax.ppermute((message, pre_grad), "wc", swap)
    sib_feats = lax.dynamic_slice_in_dim(feats, (wide_pos + 1 - 2 * core) * share_rows, share_rows, 0)
    pair_rows = jnp.where(
        core == 0,
        jnp.concatenate([message, sib_message]),
        jnp.concatenate([node_feats, sib_feats]),
    )
    pair_grad = jnp.concatenate([pre_grad, sib_pre_grad])
    half_sum = jnp.einsum("na,nb->ab", pair_rows, pair_grad, preferred_element_type=jnp.float32)
    pieces = lax.all_to_all(
        half_sum.astype(jnp.bfloat16).reshape(peers, -1, feat_width), others, 0, 0, tiled=True
    )
    reduced = jnp.sum(pieces.astype(jnp.float32), axis=0).astype(jnp.bfloat16)
    logit_hi = logits.astype(jnp.bfloat16)
    logit_rest = logits - logit_hi.astype(jnp.float32)
    logit_mid = logit_rest.astype(jnp.bfloat16)
    logit_lo = (logit_rest - logit_mid.astype(jnp.float32)).astype(jnp.bfloat16)
    logit_parts = jnp.concatenate([logit_hi, logit_mid, logit_lo]).reshape(reduced.shape[0], -1)
    payload = jnp.concatenate([reduced, logit_parts], axis=1)
    gathered = lax.all_to_all(jnp.tile(payload, (peers, 1)), others, 0, 0, tiled=True)
    own_grad, own_parts = gathered[:, :feat_width], gathered[:, feat_width:]
    sib_grad, sib_parts = lax.ppermute((own_grad, own_parts), "wc", swap)
    grad_msg = jnp.where(core == 0, own_grad, sib_grad)
    grad_self = jnp.where(core == 0, sib_grad, own_grad)
    by_core = jnp.where(core == 0, jnp.stack([own_parts, sib_parts]), jnp.stack([sib_parts, own_parts]))
    parts = by_core.reshape(
        2, lax.axis_size("wy"), lax.axis_size("wz"), lax.axis_size("loop"), 3, share_rows
    )
    parts = lax.dynamic_index_in_dim(parts, lax.axis_index("loop"), 3, keepdims=False)
    parts = jnp.transpose(parts, (1, 2, 0, 3, 4)).astype(jnp.float32)
    out_logits = (parts[:, :, :, 0] + parts[:, :, :, 1] + parts[:, :, :, 2]).reshape(-1)
    return (out_logits, grad_msg, grad_self)


def solution(mesh):
    wide_devices, loop_devices = mesh.devices.shape
    split = Mesh(mesh.devices.reshape(wide_devices // 4, 2, 2, loop_devices), (*WIDE, "loop"))
    placed = (
        P("loop", None),
        P("loop", WIDE, None, None, None),
        P("loop", WIDE, None),
        P("loop", WIDE, None),
        P("loop", WIDE),
        P(),
        P(),
        P(),
        P("loop"),
    )
    return jax.shard_map(
        body, mesh=split, in_specs=placed, out_specs=(P("loop"), P(), P()), check_vma=False
    )
```
